256 devices in a mesh: dp: 8 (over x, core), expert: 32 (over z, y).
Axes of the slice: x: 4, y: 4, z: 8, core: 2. Of those that a mesh axis runs over, the one named last changes fastest.
Arguments:
- tokens: bfloat16 [12288, 2048], P(('dp', 'expert')), may hold values from -6 to 6
- grad_out: bfloat16 [12288, 2048], P(('dp', 'expert')), may hold values from -6 to 6
- expert_ids: int32 [12288, 8], P(('dp', 'expert')), may hold values from 0 to 31, all different within a row; in each aligned block of 48 rows (0 to 47, 48 to 95, ...) at most 13 rows name the same one
- combine: float32 [12288, 8], P(('dp', 'expert')), may hold values from 0.03 to 0.5
- w_gate: bfloat16 [32, 2048, 768], P('expert'), may hold values from -0.125 to 0.125
- w_up: bfloat16 [32, 2048, 768], P('expert'), may hold values from -0.125 to 0.125
- w_down: bfloat16 [32, 768, 2048], P('expert'), may hold values from -0.21875 to 0.21875
- dither_keys: int32 [2], replicated, may hold values from 0 to 999999999
Outputs:
- grad_tokens: bfloat16 [12288, 2048], P(('dp', 'expert'))
- grad_combine: bfloat16 [12288, 8], P(('dp', 'expert'))
- grad_gate: bfloat16 [32, 2048, 768], P('expert', 'dp')
- grad_up: bfloat16 [32, 2048, 768], P('expert', 'dp')
- grad_down: bfloat16 [32, 768, 2048], P('expert', None, 'dp')
The draws below stay inside these ranges and needn't reach their ends.
Inputs may be any that keep to these rules, and one draw needn't show every extreme that they name: `expert_ids`: in the rows of one device no expert is named more than 13 times, a bound that some block reaches; the 8 experts of a token differ; every expert is named somewhere.
All inputs are finite; a program needn't handle non-finite values.
Results may differ from the reference program's by a relative error of at most 0.017.
Values may be sent and summed in bfloat16 or wider, within the bound.
No kernel may reach another device: no remote copies, remote signals or barrier semaphores. Data moves between devices by JAX's collectives and lax.ppermute only.
A program may use at most 128 MiB of HBM per device.

```python
import math
import jax
import jax.numpy as jnp
import numpy as np
from jax import lax

D = 2048
F = 768
TOP = 8
TOK_DEV = 48
EXPERTS = 32
CAP = 13
TOKENS = 12288
N_DP = 8


def levels(own_key, dims, split, smallest, largest):
    level, own = 1.0, jax.random.fold_in(own_key, 6)
    for dim, blocks in split:
        steps = jnp.exp(jax.random.uniform(jax.random.fold_in(own, dim), (blocks,), jnp.float32, smallest / len(split), largest / len(split)))
        level = level * jnp.repeat(steps, dims[dim] // blocks).reshape([-1 if axis == dim else 1 for axis in range(len(dims))])
    return level


def assign_block(rng, own, number, rows, amount, top, reach, slope):
    order = jax.random.permutation(rng, amount)
    packed, usual = load_shares(amount, rows * top, reach, slope, True), load_shares(amount, rows * top, reach, slope, False)
    places = jnp.arange(amount)

    def named(tallies, offset_by):
        used = int((tallies > 0).sum())
        fixed = max(1, used // 4)
        shifted = fixed + (places - fixed + offset_by * (used - fixed)) % max(1, amount - fixed)
        return jnp.zeros((amount,), jnp.int32).at[order[jnp.where(places < fixed, places, shifted)]].set(jnp.asarray(tallies, jnp.int32))

    tallies = jnp.where(number % 4 == 0, named(packed, number // 4), named(usual, number - number // 4 - 1))
    mixed = jax.random.permutation(jax.random.fold_in(own, 3), amount)
    donor, sink = mixed[0:amount // 2 * 2:2], mixed[1:amount // 2 * 2:2]
    room = jnp.minimum(tallies[donor] - 1, reach - tallies[sink]) // 2
    room = jnp.where((donor == order[0]) | (sink == order[0]) | (tallies[sink] == 0), 0, jnp.maximum(room, 0))
    shifted = jax.random.randint(jax.random.fold_in(own, 4), (amount // 2,), 0, 1 << 20) % (room + 1)
    tallies = tallies.at[donor].add(-shifted).at[sink].add(shifted)
    labels = jnp.searchsorted(jnp.cumsum(tallies), jnp.arange(rows * top), side="right").astype(jnp.int32)
    table = labels.reshape(top, rows).T
    table = table[jax.random.permutation(jax.random.fold_in(own, 1), rows)]
    offset_by = jax.random.randint(jax.random.fold_in(own, 2), (rows, 1), 0, top)
    return jnp.take_along_axis(table, (jnp.arange(top)[None, :] + offset_by) % top, axis=1)


def load_shares(amount, total, most, skew, full):
    portions = [(1 << 20) // math.isqrt(grade ** skew) + 1 for grade in range(1, amount + 1)]
    largest = most if full else min(most, max(-(-total // amount), total * portions[0] // sum(portions)))
    least = 1 if total - largest >= amount - 1 else 0
    given, spare = [largest] + [least] * (amount - 1), total - largest - least * (amount - 1)
    while spare > 0:
        movable = [i for i in range(1, amount) if given[i] < largest] or [i for i in range(1, amount) if given[i] < most]
        whole, budget = sum([portions[i] for i in movable]), spare
        for i in movable:
            extra = min(most - given[i], max(1, budget * portions[i] // whole), spare)
            given[i] = given[i] + extra
            spare = spare - extra
    return np.array(given)


def scatter_about(stream_key, shape, width, bound, pieces=(), held_as=jnp.bfloat16):
    entries = width * jax.random.normal(stream_key, shape, jnp.float32)
    if pieces:
        entries = entries * levels(stream_key, shape, pieces, -0.22, 0.18)
    return jnp.clip(entries, -bound, bound).astype(held_as)


def setup_inputs(seed: int = 0) -> dict:
    splits = jax.random.split(jax.random.key(seed), 9)
    tokens = scatter_about(splits[0], (TOKENS, D), 1.0, 6.0, ((0, 256),))
    grad_out = scatter_about(splits[1], (TOKENS, D), 1.0, 6.0, ((0, 256),))
    expert_ids_keys = jax.random.split(jax.random.fold_in(splits[2], 1), TOKENS // TOK_DEV)
    expert_ids_turns = jax.random.permutation(jax.random.fold_in(splits[2], 3), TOKENS // TOK_DEV)
    expert_ids = jax.vmap(lambda own, number: assign_block(jax.random.fold_in(splits[2], 2), own, number, TOK_DEV, EXPERTS, TOP, CAP, 1))(expert_ids_keys, expert_ids_turns).reshape((TOKENS, TOP))
    combine = jnp.clip(jnp.exp(math.log(0.5) - 2.8134107 * jax.random.uniform(splits[3], (TOKENS, TOP), jnp.float32) ** levels(splits[3], (TOKENS, TOP), ((0, 256),), -0.2, 0.2)), 0.03, 0.5)
    w_gate = scatter_about(splits[4], (EXPERTS, D, F), D ** -0.5, 0.125, ((0, 32),))
    w_up = scatter_about(splits[5], (EXPERTS, D, F), D ** -0.5, 0.125, ((0, 32),))
    w_down = scatter_about(splits[6], (EXPERTS, F, D), F ** -0.5, 0.21875, ((0, 32),))
    dither_keys = jax.random.randint(splits[7], (2,), 0, 1000000000).astype(jnp.int32)
    return dict(tokens=tokens, grad_out=grad_out, expert_ids=expert_ids, combine=combine, w_gate=w_gate, w_up=w_up, w_down=w_down, dither_keys=dither_keys)


def mix_bits(hashed):
    hashed = jnp.bitwise_xor(hashed, jnp.bitwise_and(jnp.right_shift(hashed, 16), 65535))
    hashed = hashed * 2146121005
    hashed = jnp.bitwise_xor(hashed, jnp.bitwise_and(jnp.right_shift(hashed, 15), 131071))
    hashed = hashed * 1284865837
    hashed = jnp.bitwise_xor(hashed, jnp.bitwise_and(jnp.right_shift(hashed, 16), 65535))
    return hashed


def dither(row_block, tok_index, key_word):
    columns = jnp.arange(row_block.shape[1], dtype=jnp.int32)
    salted = mix_bits(key_word + 977)
    keyed_hash = mix_bits(jnp.bitwise_xor(tok_index[:, None] * 4099 + columns[None, :], salted))
    uniform_val = jnp.bitwise_and(keyed_hash, 65535).astype(jnp.float32) * (1.0 / 65536.0)
    values = row_block.astype(jnp.float32)
    magnitude = jnp.abs(values)
    spacing = jnp.full(magnitude.shape, 2.0 ** -9, jnp.float32)
    for power in range(-5, 9):
        spacing = jnp.where(magnitude >= 2.0 ** power, spacing * 2.0, spacing)
    rounded = jnp.floor(magnitude / spacing + uniform_val) * spacing
    return jnp.where(values < 0, -rounded, rounded).astype(jnp.bfloat16)


def settle(partial_value):
    return lax.optimization_barrier(partial_value.astype(jnp.bfloat16)).astype(jnp.float32)


def reference(tokens, grad_out, expert_ids, combine, w_gate, w_up, w_down, dither_keys):
    token_count, model_width = tokens.shape
    tok_index = jnp.arange(token_count, dtype=jnp.int32)
    x_dith = dither(tokens, tok_index, dither_keys[0])
    g_dith = dither(grad_out, tok_index, dither_keys[1])
    blocks = token_count // TOK_DEV
    per_block = TOK_DEV * TOP
    block_slots = EXPERTS * CAP
    route_ids = expert_ids.reshape(blocks, per_block)
    onehot = (route_ids[:, :, None] == jnp.arange(EXPERTS, dtype=jnp.int32)[None, None, :]).astype(jnp.int32)
    position = jnp.sum((jnp.cumsum(onehot, axis=1) - 1) * onehot, axis=2)
    flat_slot = (jnp.arange(blocks, dtype=jnp.int32)[:, None] * block_slots + route_ids * CAP + position).reshape(-1)
    pair_total = blocks * per_block
    pair_table = jnp.full((blocks * block_slots,), pair_total, jnp.int32)
    pair_table = pair_table.at[flat_slot].set(jnp.arange(pair_total, dtype=jnp.int32))
    pair_table = pair_table.reshape(N_DP, EXPERTS, EXPERTS, CAP).transpose(2, 0, 1, 3).reshape(EXPERTS, N_DP, EXPERTS * CAP)
    weight_bf = lax.optimization_barrier(combine.astype(jnp.bfloat16)).astype(jnp.float32).reshape(-1)
    weight_pad = jnp.concatenate([weight_bf, jnp.zeros((1,), jnp.float32)])
    x_pad = jnp.concatenate([x_dith, jnp.zeros((1, model_width), jnp.bfloat16)], axis=0)
    g_pad = jnp.concatenate([g_dith, jnp.zeros((1, model_width), jnp.bfloat16)], axis=0)

    def expert_step(totals, inputs):
        grad_acc, comb_acc = totals
        pair_slice, gate_w, up_w, down_w = inputs
        hidden_units = gate_w.shape[1]
        gate_sum = jnp.zeros((model_width, hidden_units), jnp.float32)
        up_sum = jnp.zeros((model_width, hidden_units), jnp.float32)
        down_sum = jnp.zeros((hidden_units, model_width), jnp.float32)
        for dp_group in range(N_DP):
            pair_ids = pair_slice[dp_group]
            row_tok = pair_ids // TOP
            row_x = x_pad[row_tok]
            row_g = g_pad[row_tok]
            weight = weight_pad[pair_ids][:, None]
            gate_pre = jnp.dot(row_x, gate_w, preferred_element_type=jnp.float32)
            up_pre = jnp.dot(row_x, up_w, preferred_element_type=jnp.float32)
            sigmoid_val = jax.nn.sigmoid(gate_pre)
            silu_val = gate_pre * sigmoid_val
            hidden = (silu_val * up_pre).astype(jnp.bfloat16)
            back_grad = jnp.dot(row_g, down_w.T, preferred_element_type=jnp.float32)
            comb_slot = jnp.sum(hidden.astype(jnp.float32) * back_grad, axis=1).astype(jnp.bfloat16)
            hidden_grad = weight * back_grad
            gate_rows_grad = (hidden_grad * up_pre * sigmoid_val * (1.0 + gate_pre * (1.0 - sigmoid_val))).astype(jnp.bfloat16)
            up_rows_grad = (hidden_grad * silu_val).astype(jnp.bfloat16)
            scaled_grad = (weight * row_g.astype(jnp.float32)).astype(jnp.bfloat16)
            gate_sum = gate_sum + settle(jnp.dot(row_x.T, gate_rows_grad, preferred_element_type=jnp.float32))
            up_sum = up_sum + settle(jnp.dot(row_x.T, up_rows_grad, preferred_element_type=jnp.float32))
            down_sum = down_sum + settle(jnp.dot(hidden.T, scaled_grad, preferred_element_type=jnp.float32))
            row_grad = (jnp.dot(gate_rows_grad, gate_w.T, preferred_element_type=jnp.float32) + jnp.dot(up_rows_grad, up_w.T, preferred_element_type=jnp.float32)).astype(jnp.bfloat16)
            grad_acc = grad_acc.at[row_tok].add(row_grad.astype(jnp.float32))
            comb_acc = comb_acc.at[pair_ids].set(comb_slot.astype(jnp.float32))
        return (grad_acc, comb_acc), (gate_sum.astype(jnp.bfloat16), up_sum.astype(jnp.bfloat16), down_sum.astype(jnp.bfloat16))

    initial = (jnp.zeros((token_count + 1, model_width), jnp.float32), jnp.zeros((pair_total + 1,), jnp.float32))
    (grad_acc, comb_acc), (grad_gate, grad_up, grad_down) = lax.scan(expert_step, initial, (pair_table, w_gate, w_up, w_down))
    grad_tokens = grad_acc[:token_count].astype(jnp.bfloat16)
    grad_combine = comb_acc[:pair_total].reshape(token_count, TOP).astype(jnp.bfloat16)
    return grad_tokens, grad_combine, grad_gate, grad_up, grad_down
```

```python
import jax
import jax.numpy as jnp
from jax import lax
from jax.sharding import PartitionSpec as P


def mix_bits(hashed):
    hashed = jnp.bitwise_xor(hashed, jnp.bitwise_and(jnp.right_shift(hashed, 16), 65535))
    hashed = hashed * 2146121005
    hashed = jnp.bitwise_xor(hashed, jnp.bitwise_and(jnp.right_shift(hashed, 15), 131071))
    hashed = hashed * 1284865837
    hashed = jnp.bitwise_xor(hashed, jnp.bitwise_and(jnp.right_shift(hashed, 16), 65535))
    return hashed


def dither(row_block, tok_index, key_word):
    columns = jnp.arange(row_block.shape[1], dtype=jnp.int32)
    salted = mix_bits(key_word + 977)
    keyed_hash = mix_bits(jnp.bitwise_xor(tok_index[:, None] * 4099 + columns[None, :], salted))
    uniform_val = jnp.bitwise_and(keyed_hash, 65535).astype(jnp.float32) * (1.0 / 65536.0)
    values = row_block.astype(jnp.float32)
    magnitude = jnp.abs(values)
    spacing = jnp.full(magnitude.shape, 2.0 ** (-9), jnp.float32)
    for power in range(-5, 9):
        spacing = jnp.where(magnitude >= 2.0**power, spacing * 2.0, spacing)
    rounded = jnp.floor(magnitude / spacing + uniform_val) * spacing
    return jnp.where(values < 0, -rounded, rounded).astype(jnp.bfloat16)


def body(tokens, grad_out, expert_ids, combine, w_gate, w_up, w_down, dither_keys):
    tok_dev, model_width = tokens.shape
    fan_out = expert_ids.shape[1]
    owners = lax.axis_size("expert")
    capacity = 9 * tok_dev * fan_out // (8 * owners)
    slot_count = owners * capacity
    lane = 128
    source_block = lax.axis_index("dp") * owners + lax.axis_index("expert")
    tok_index = source_block * tok_dev + jnp.arange(tok_dev, dtype=jnp.int32)
    x_dith = dither(tokens, tok_index, dither_keys[0])
    g_dith = dither(grad_out, tok_index, dither_keys[1])
    flat_ids = expert_ids.reshape(-1)
    onehot = (flat_ids[:, None] == jnp.arange(owners, dtype=jnp.int32)[None, :]).astype(jnp.int32)
    position = jnp.sum((jnp.cumsum(onehot, axis=0) - 1) * onehot, axis=1)
    slot_index = flat_ids * capacity + position
    pair_rows = jnp.arange(tok_dev * fan_out, dtype=jnp.int32)
    source_row = (
        jnp.full((slot_count,), tok_dev, jnp.int32).at[slot_index].set(pair_rows // fan_out)
    )
    slot_weight = (
        jnp.zeros((slot_count,), jnp.bfloat16)
        .at[slot_index]
        .set(combine.reshape(-1).astype(jnp.bfloat16))
    )
    token_table = jnp.concatenate(
        [
            jnp.concatenate([x_dith, g_dith], axis=1),
            jnp.zeros((1, 2 * model_width), jnp.bfloat16),
        ],
        axis=0,
    )
    weight_cols = jnp.pad(slot_weight[:, None], ((0, 0), (0, lane - 1)))
    send = jnp.concatenate([token_table[source_row], weight_cols], axis=1)
    recv = lax.all_to_all(
        send.reshape(owners, capacity, send.shape[1]), "expert", split_axis=0, concat_axis=0, tiled=True
    ).reshape(slot_count, send.shape[1])
    row_x = recv[:, :model_width]
    row_g = recv[:, model_width : 2 * model_width]
    weight = recv[:, 2 * model_width : 2 * model_width + 1].astype(jnp.float32)
    gate_w = w_gate[0]
    up_w = w_up[0]
    down_w = w_down[0]
    gate_pre = jnp.dot(row_x, gate_w, preferred_element_type=jnp.float32)
    up_pre = jnp.dot(row_x, up_w, preferred_element_type=jnp.float32)
    sigmoid_val = jax.nn.sigmoid(gate_pre)
    silu_val = gate_pre * sigmoid_val
    hidden = (silu_val * up_pre).astype(jnp.bfloat16)
    back_grad = jnp.dot(row_g, down_w.T, preferred_element_type=jnp.float32)
    comb_slot = jnp.sum(hidden.astype(jnp.float32) * back_grad, axis=1).astype(jnp.bfloat16)
    hidden_grad = weight * back_grad
    gate_rows_grad = (
        hidden_grad * up_pre * sigmoid_val * (1.0 + gate_pre * (1.0 - sigmoid_val))
    ).astype(jnp.bfloat16)
    up_rows_grad = (hidden_grad * silu_val).astype(jnp.bfloat16)
    scaled_grad = (weight * row_g.astype(jnp.float32)).astype(jnp.bfloat16)
    gate_part = jnp.dot(row_x.T, gate_rows_grad, preferred_element_type=jnp.float32)
    up_part = jnp.dot(row_x.T, up_rows_grad, preferred_element_type=jnp.float32)
    down_part_t = jnp.dot(scaled_grad.T, hidden, preferred_element_type=jnp.float32)
    hidden_units = gate_w.shape[1]
    parts = jnp.concatenate(
        [gate_part.astype(jnp.bfloat16), up_part.astype(jnp.bfloat16), down_part_t.astype(jnp.bfloat16)],
        axis=1,
    )
    reduced = lax.psum_scatter(parts, "dp", scatter_dimension=0, tiled=True)
    row_grad = (
        jnp.dot(gate_rows_grad, gate_w.T, preferred_element_type=jnp.float32)
        + jnp.dot(up_rows_grad, up_w.T, preferred_element_type=jnp.float32)
    ).astype(jnp.bfloat16)
    back_send = jnp.concatenate(
        [row_grad, jnp.pad(comb_slot[:, None], ((0, 0), (0, lane - 1)))], axis=1
    )
    back = lax.all_to_all(
        back_send.reshape(owners, capacity, back_send.shape[1]),
        "expert",
        split_axis=0,
        concat_axis=0,
        tiled=True,
    ).reshape(slot_count, back_send.shape[1])
    back_flat = back[slot_index]
    grad_tokens = jnp.sum(
        back_flat[:, :model_width].reshape(tok_dev, fan_out, model_width).astype(jnp.float32), axis=1
    ).astype(jnp.bfloat16)
    grad_combine = back_flat[:, model_width].reshape(tok_dev, fan_out)
    gate_grad = reduced[:, :hidden_units]
    up_grad = reduced[:, hidden_units : 2 * hidden_units]
    down_grad = reduced[:, 2 * hidden_units :].T
    return (
        grad_tokens,
        grad_combine,
        gate_grad[None],
        up_grad[None],
        down_grad[None],
    )


def solution(mesh):
    return jax.shard_map(
        body,
        mesh=mesh,
        in_specs=(
            P(("dp", "expert"), None),
            P(("dp", "expert"), None),
            P(("dp", "expert"), None),
            P(("dp", "expert"), None),
            P("expert", None, None),
            P("expert", None, None),
            P("expert", None, None),
            P(),
        ),
        out_specs=(
            P(("dp", "expert"), None),
            P(("dp", "expert"), None),
            P("expert", "dp", None),
            P("expert", "dp", None),
            P("expert", None, "dp"),
        ),
        check_vma=False,
    )
```

```python
import jax
import jax.numpy as jnp
from jax import lax
from jax.sharding import PartitionSpec as P


def mix_bits(hashed):
    hashed = jnp.bitwise_xor(hashed, jnp.bitwise_and(jnp.right_shift(hashed, 16), 65535))
    hashed = hashed * 2146121005
    hashed = jnp.bitwise_xor(hashed, jnp.bitwise_and(jnp.right_shift(hashed, 15), 131071))
    hashed = hashed * 1284865837
    hashed = jnp.bitwise_xor(hashed, jnp.bitwise_and(jnp.right_shift(hashed, 16), 65535))
    return hashed


def dither(row_block, tok_index, key_word):
    columns = jnp.arange(row_block.shape[1], dtype=jnp.int32)
    salted = mix_bits(key_word + 977)
    keyed_hash = mix_bits(jnp.bitwise_xor(tok_index[:, None] * 4099 + columns[None, :], salted))
    uniform_val = jnp.bitwise_and(keyed_hash, 65535).astype(jnp.float32) * (1.0 / 65536.0)
    values = row_block.astype(jnp.float32)
    magnitude = jnp.abs(values)
    spacing = jnp.full(magnitude.shape, 2.0 ** (-9), jnp.float32)
    for power in range(-5, 9):
        spacing = jnp.where(magnitude >= 2.0**power, spacing * 2.0, spacing)
    rounded = jnp.floor(magnitude / spacing + uniform_val) * spacing
    return jnp.where(values < 0, -rounded, rounded).astype(jnp.bfloat16)


def to_wire(rows, scalars, owners):
    capacity = rows.shape[0] // owners
    body_len = capacity * rows.shape[1]
    tile = 16 * 128
    total = -(-(body_len + capacity) // tile) * tile
    flat = jnp.concatenate(
        [
            rows.reshape(owners, body_len),
            scalars.reshape(owners, capacity).astype(rows.dtype),
            jnp.zeros((owners, total - body_len - capacity), rows.dtype),
        ],
        axis=1,
    )
    return flat.reshape(owners, 16, total // 16)


def from_wire(wire, owners, capacity, width):
    flat = wire.reshape(owners, -1)
    body_len = capacity * width
    return flat[:, :body_len].reshape(owners * capacity, width), flat[:, body_len : body_len + capacity].reshape(-1)


def body(tokens, grad_out, expert_ids, combine, w_gate, w_up, w_down, dither_keys):
    tok_dev, model_width = tokens.shape
    fan_out = expert_ids.shape[1]
    owners = lax.axis_size("expert")
    capacity = 9 * tok_dev * fan_out // (8 * owners)
    slot_count = owners * capacity
    source_block = lax.axis_index("dp") * owners + lax.axis_index("expert")
    tok_index = source_block * tok_dev + jnp.arange(tok_dev, dtype=jnp.int32)
    x_dith = dither(tokens, tok_index, dither_keys[0])
    g_dith = dither(grad_out, tok_index, dither_keys[1])
    flat_ids = expert_ids.reshape(-1)
    onehot = (flat_ids[:, None] == jnp.arange(owners, dtype=jnp.int32)[None, :]).astype(jnp.int32)
    position = jnp.sum((jnp.cumsum(onehot, axis=0) - 1) * onehot, axis=1)
    slot_index = flat_ids * capacity + position
    pair_rows = jnp.arange(tok_dev * fan_out, dtype=jnp.int32)
    source_row = (
        jnp.full((slot_count,), tok_dev, jnp.int32).at[slot_index].set(pair_rows // fan_out)
    )
    slot_weight = (
        jnp.zeros((slot_count,), jnp.bfloat16)
        .at[slot_index]
        .set(combine.reshape(-1).astype(jnp.bfloat16))
    )
    token_table = jnp.concatenate(
        [
            jnp.concatenate([x_dith, g_dith], axis=1),
            jnp.zeros((1, 2 * model_width), jnp.bfloat16),
        ],
        axis=0,
    )
    wire = lax.all_to_all(
        to_wire(token_table[source_row], slot_weight, owners), "expert", split_axis=0, concat_axis=0, tiled=True
    )
    recv, recv_weight = from_wire(wire, owners, capacity, 2 * model_width)
    row_x = recv[:, :model_width]
    row_g = recv[:, model_width : 2 * model_width]
    weight = recv_weight[:, None].astype(jnp.float32)
    gate_w = w_gate[0]
    up_w = w_up[0]
    down_w = w_down[0]
    gate_pre = jnp.dot(row_x, gate_w, preferred_element_type=jnp.float32)
    up_pre = jnp.dot(row_x, up_w, preferred_element_type=jnp.float32)
    sigmoid_val = jax.nn.sigmoid(gate_pre)
    silu_val = gate_pre * sigmoid_val
    hidden = (silu_val * up_pre).astype(jnp.bfloat16)
    back_grad = jnp.dot(row_g, down_w.T, preferred_element_type=jnp.float32)
    comb_slot = jnp.sum(hidden.astype(jnp.float32) * back_grad, axis=1).astype(jnp.bfloat16)
    hidden_grad = weight * back_grad
    gate_rows_grad = (
        hidden_grad * up_pre * sigmoid_val * (1.0 + gate_pre * (1.0 - sigmoid_val))
    ).astype(jnp.bfloat16)
    up_rows_grad = (hidden_grad * silu_val).astype(jnp.bfloat16)
    scaled_grad = (weight * row_g.astype(jnp.float32)).astype(jnp.bfloat16)
    gate_part = jnp.dot(row_x.T, gate_rows_grad, preferred_element_type=jnp.float32)
    up_part = jnp.dot(row_x.T, up_rows_grad, preferred_element_type=jnp.float32)
    down_part_t = jnp.dot(scaled_grad.T, hidden, preferred_element_type=jnp.float32)
    hidden_units = gate_w.shape[1]
    parts = jnp.concatenate(
        [gate_part.astype(jnp.bfloat16), up_part.astype(jnp.bfloat16), down_part_t.astype(jnp.bfloat16)],
        axis=1,
    )
    reduced = lax.psum_scatter(parts, "dp", scatter_dimension=0, tiled=True)
    row_grad = (
        jnp.dot(gate_rows_grad, gate_w.T, preferred_element_type=jnp.float32)
        + jnp.dot(up_rows_grad, up_w.T, preferred_element_type=jnp.float32)
    ).astype(jnp.bfloat16)
    back_wire = lax.all_to_all(
        to_wire(row_grad, comb_slot, owners), "expert", split_axis=0, concat_axis=0, tiled=True
    )
    back_rows, back_comb = from_wire(back_wire, owners, capacity, model_width)
    grad_tokens = jnp.sum(
        back_rows[slot_index].reshape(tok_dev, fan_out, model_width).astype(jnp.float32), axis=1
    ).astype(jnp.bfloat16)
    grad_combine = back_comb[slot_index].reshape(tok_dev, fan_out)
    gate_grad = reduced[:, :hidden_units]
    up_grad = reduced[:, hidden_units : 2 * hidden_units]
    down_grad = reduced[:, 2 * hidden_units :].T
    return (
        grad_tokens,
        grad_combine,
        gate_grad[None],
        up_grad[None],
        down_grad[None],
    )


def solution(mesh):
    return jax.shard_map(
        body,
        mesh=mesh,
        in_specs=(
            P(("dp", "expert"), None),
            P(("dp", "expert"), None),
            P(("dp", "expert"), None),
            P(("dp", "expert"), None),
            P("expert", None, None),
            P("expert", None, None),
            P("expert", None, None),
            P(),
        ),
        out_specs=(
            P(("dp", "expert"), None),
            P(("dp", "expert"), None),
            P("expert", "dp", None),
            P("expert", "dp", None),
            P("expert", None, "dp"),
        ),
        check_vma=False,
    )
```

```python
import jax
import jax.numpy as jnp
from jax import lax
from jax.sharding import PartitionSpec as P


def mix_bits(hashed):
    hashed = jnp.bitwise_xor(hashed, jnp.bitwise_and(jnp.right_shift(hashed, 16), 65535))
    hashed = hashed * 2146121005
    hashed = jnp.bitwise_xor(hashed, jnp.bitwise_and(jnp.right_shift(hashed, 15), 131071))
    hashed = hashed * 1284865837
    hashed = jnp.bitwise_xor(hashed, jnp.bitwise_and(jnp.right_shift(hashed, 16), 65535))
    return hashed


def dither(row_block, tok_index, key_word):
    columns = jnp.arange(row_block.shape[1], dtype=jnp.int32)
    salted = mix_bits(key_word + 977)
    keyed_hash = mix_bits(jnp.bitwise_xor(tok_index[:, None] * 4099 + columns[None, :], salted))
    uniform_val = jnp.bitwise_and(keyed_hash, 65535).astype(jnp.float32) * (1.0 / 65536.0)
    values = row_block.astype(jnp.float32)
    magnitude = jnp.abs(values)
    spacing = jnp.full(magnitude.shape, 2.0 ** (-9), jnp.float32)
    for power in range(-5, 9):
        spacing = jnp.where(magnitude >= 2.0**power, spacing * 2.0, spacing)
    rounded = jnp.floor(magnitude / spacing + uniform_val) * spacing
    return jnp.where(values < 0, -rounded, rounded).astype(jnp.bfloat16)


def body(tokens, grad_out, expert_ids, combine, w_gate, w_up, w_down, dither_keys):
    tok_dev, model_width = tokens.shape
    fan_out = expert_ids.shape[1]
    owners = lax.axis_size("expert")
    capacity = 9 * tok_dev * fan_out // (8 * owners)
    slot_count = owners * capacity
    lanes = 128
    tile_rows = model_width // lanes
    source_block = lax.axis_index("dp") * owners + lax.axis_index("expert")
    tok_index = source_block * tok_dev + jnp.arange(tok_dev, dtype=jnp.int32)
    x_dith = dither(tokens, tok_index, dither_keys[0])
    g_dith = dither(grad_out, tok_index, dither_keys[1])
    flat_ids = expert_ids.reshape(-1)
    onehot = (flat_ids[:, None] == jnp.arange(owners, dtype=jnp.int32)[None, :]).astype(jnp.int32)
    position = jnp.sum((jnp.cumsum(onehot, axis=0) - 1) * onehot, axis=1)
    slot_index = flat_ids * capacity + position
    pair_rows = jnp.arange(tok_dev * fan_out, dtype=jnp.int32)
    hit = slot_index[:, None] == jnp.arange(slot_count, dtype=jnp.int32)[None, :]
    source_row = jnp.min(jnp.where(hit, (pair_rows // fan_out)[:, None], tok_dev), axis=0)
    slot_weight = jnp.sum(
        jnp.where(hit, combine.reshape(-1).astype(jnp.bfloat16).astype(jnp.float32)[:, None], 0.0), axis=0
    ).astype(jnp.bfloat16)
    empty_tile = jnp.zeros((1, tile_rows, lanes), jnp.bfloat16)
    weight_tiles = jnp.pad(
        slot_weight.reshape(owners, 1, capacity), ((0, 0), (0, tile_rows - 1), (0, lanes - capacity))
    )
    table = jnp.concatenate(
        [
            x_dith.reshape(tok_dev, tile_rows, lanes),
            empty_tile,
            g_dith.reshape(tok_dev, tile_rows, lanes),
            empty_tile,
            weight_tiles,
        ],
        axis=0,
    )
    rows_by_dest = source_row.reshape(owners, capacity)
    weight_base = 2 * (tok_dev + 1)
    tile_index = jnp.concatenate(
        [
            rows_by_dest,
            rows_by_dest + (tok_dev + 1),
            weight_base + jnp.arange(owners, dtype=jnp.int32)[:, None],
        ],
        axis=1,
    )
    wire = lax.all_to_all(table[tile_index], "expert", split_axis=0, concat_axis=0, tiled=True)
    row_x = wire[:, :capacity].reshape(slot_count, model_width)
    row_g = wire[:, capacity : 2 * capacity].reshape(slot_count, model_width)
    weight = wire[:, 2 * capacity, 0, :capacity].reshape(slot_count, 1).astype(jnp.float32)
    gate_w = w_gate[0]
    up_w = w_up[0]
    down_w = w_down[0]
    gate_pre = jnp.dot(row_x, gate_w, preferred_element_type=jnp.float32)
    up_pre = jnp.dot(row_x, up_w, preferred_element_type=jnp.float32)
    sigmoid_val = jax.nn.sigmoid(gate_pre)
    silu_val = gate_pre * sigmoid_val
    hidden = (silu_val * up_pre).astype(jnp.bfloat16)
    back_grad = jnp.dot(row_g, down_w.T, preferred_element_type=jnp.float32)
    comb_slot = jnp.sum(hidden.astype(jnp.float32) * back_grad, axis=1).astype(jnp.bfloat16)
    hidden_grad = weight * back_grad
    gate_rows_grad = (
        hidden_grad * up_pre * sigmoid_val * (1.0 + gate_pre * (1.0 - sigmoid_val))
    ).astype(jnp.bfloat16)
    up_rows_grad = (hidden_grad * silu_val).astype(jnp.bfloat16)
    scaled_grad = (weight * row_g.astype(jnp.float32)).astype(jnp.bfloat16)
    gate_part = jnp.dot(row_x.T, gate_rows_grad, preferred_element_type=jnp.float32)
    up_part = jnp.dot(row_x.T, up_rows_grad, preferred_element_type=jnp.float32)
    down_part_t = jnp.dot(scaled_grad.T, hidden, preferred_element_type=jnp.float32)
    hidden_units = gate_w.shape[1]
    parts = jnp.concatenate(
        [gate_part.astype(jnp.bfloat16), up_part.astype(jnp.bfloat16), down_part_t.astype(jnp.bfloat16)],
        axis=1,
    )
    reduced = lax.psum_scatter(parts, "dp", scatter_dimension=0, tiled=True)
    row_grad = (
        jnp.dot(gate_rows_grad, gate_w.T, preferred_element_type=jnp.float32)
        + jnp.dot(up_rows_grad, up_w.T, preferred_element_type=jnp.float32)
    ).astype(jnp.bfloat16)
    comb_tile = jnp.pad(
        comb_slot.reshape(owners, 1, 1, capacity), ((0, 0), (0, 0), (0, tile_rows - 1), (0, lanes - capacity))
    )
    back_send = jnp.concatenate(
        [row_grad.reshape(owners, capacity, tile_rows, lanes), comb_tile], axis=1
    )
    back = lax.all_to_all(back_send, "expert", split_axis=0, concat_axis=0, tiled=True)
    back_rows = back[:, :capacity].reshape(slot_count, tile_rows, lanes)
    back_comb = back[:, capacity, 0, :capacity].reshape(slot_count)
    grad_tokens = (
        jnp.sum(back_rows[slot_index].reshape(tok_dev, fan_out, tile_rows, lanes).astype(jnp.float32), axis=1)
        .astype(jnp.bfloat16)
        .reshape(tok_dev, model_width)
    )
    grad_combine = back_comb[slot_index].reshape(tok_dev, fan_out)
    gate_grad = reduced[:, :hidden_units]
    up_grad = reduced[:, hidden_units : 2 * hidden_units]
    down_grad = reduced[:, 2 * hidden_units :].T
    return (
        grad_tokens,
        grad_combine,
        gate_grad[None],
        up_grad[None],
        down_grad[None],
    )


def solution(mesh):
    return jax.shard_map(
        body,
        mesh=mesh,
        in_specs=(
            P(("dp", "expert"), None),
            P(("dp", "expert"), None),
            P(("dp", "expert"), None),
            P(("dp", "expert"), None),
            P("expert", None, None),
            P("expert", None, None),
            P("expert", None, None),
            P(),
        ),
        out_specs=(
            P(("dp", "expert"), None),
            P(("dp", "expert"), None),
            P("expert", "dp", None),
            P("expert", "dp", None),
            P("expert", None, "dp"),
        ),
        check_vma=False,
    )
```

```python
import jax
import jax.numpy as jnp
from jax import lax
from jax.sharding import PartitionSpec as P


def mix_bits(hashed):
    hashed = jnp.bitwise_xor(hashed, jnp.bitwise_and(jnp.right_shift(hashed, 16), 65535))
    hashed = hashed * 2146121005
    hashed = jnp.bitwise_xor(hashed, jnp.bitwise_and(jnp.right_shift(hashed, 15), 131071))
    hashed = hashed * 1284865837
    hashed = jnp.bitwise_xor(hashed, jnp.bitwise_and(jnp.right_shift(hashed, 16), 65535))
    return hashed


def dither(row_block, tok_index, key_word):
    columns = jnp.arange(row_block.shape[1], dtype=jnp.int32)
    salted = mix_bits(key_word + 977)
    keyed_hash = mix_bits(jnp.bitwise_xor(tok_index[:, None] * 4099 + columns[None, :], salted))
    uniform_val = jnp.bitwise_and(keyed_hash, 65535).astype(jnp.float32) * (1.0 / 65536.0)
    values = row_block.astype(jnp.float32)
    magnitude = jnp.abs(values)
    spacing = jnp.full(magnitude.shape, 2.0 ** (-9), jnp.float32)
    for power in range(-5, 9):
        spacing = jnp.where(magnitude >= 2.0**power, spacing * 2.0, spacing)
    rounded = jnp.floor(magnitude / spacing + uniform_val) * spacing
    return jnp.where(values < 0, -rounded, rounded).astype(jnp.bfloat16)


def body(tokens, grad_out, expert_ids, combine, w_gate, w_up, w_down, dither_keys):
    tok_dev, model_width = tokens.shape
    fan_out = expert_ids.shape[1]
    owners = lax.axis_size("expert")
    capacity = 9 * tok_dev * fan_out // (8 * owners)
    slot_count = owners * capacity
    lanes = 128
    tile_rows = model_width // lanes
    source_block = lax.axis_index("dp") * owners + lax.axis_index("expert")
    tok_index = source_block * tok_dev + jnp.arange(tok_dev, dtype=jnp.int32)
    x_dith = dither(tokens, tok_index, dither_keys[0])
    g_dith = dither(grad_out, tok_index, dither_keys[1])
    flat_ids = expert_ids.reshape(-1)
    onehot = (flat_ids[:, None] == jnp.arange(owners, dtype=jnp.int32)[None, :]).astype(jnp.int32)
    position = jnp.sum((jnp.cumsum(onehot, axis=0) - 1) * onehot, axis=1)
    slot_index = flat_ids * capacity + position
    pair_rows = jnp.arange(tok_dev * fan_out, dtype=jnp.int32)
    hit = slot_index[:, None] == jnp.arange(slot_count, dtype=jnp.int32)[None, :]
    source_row = jnp.min(jnp.where(hit, (pair_rows // fan_out)[:, None], tok_dev), axis=0)
    slot_weight = jnp.sum(
        jnp.where(hit, combine.reshape(-1).astype(jnp.bfloat16).astype(jnp.float32)[:, None], 0.0), axis=0
    ).astype(jnp.bfloat16)
    empty_tile = jnp.zeros((1, tile_rows, lanes), jnp.bfloat16)
    table = jnp.concatenate(
        [
            x_dith.reshape(tok_dev, tile_rows, lanes),
            empty_tile,
            g_dith.reshape(tok_dev, tile_rows, lanes),
            empty_tile,
        ],
        axis=0,
    )
    rows_by_dest = source_row.reshape(owners, capacity)
    weight_by_dest = slot_weight.reshape(owners, capacity)
    gate_w = w_gate[0]
    up_w = w_up[0]
    down_w = w_down[0]
    hidden_units = gate_w.shape[1]
    first = (capacity + 1) // 2
    chunks = ((0, first), (first, capacity - first))
    gate_acc = up_acc = down_acc = None
    back_tables = []
    back_combs = []
    sends = []
    for lo, size in chunks:
        rows = rows_by_dest[:, lo : lo + size]
        weight_tile = jnp.pad(
            weight_by_dest[:, None, lo : lo + size], ((0, 0), (0, tile_rows - 1), (0, lanes - size))
        )
        sends.append(
            jnp.concatenate([table[rows], table[rows + (tok_dev + 1)], weight_tile[:, None]], axis=1)
        )
    wire = None
    for (lo, size), send in zip(chunks, sends):
        if wire is not None:
            wire, send = lax.optimization_barrier((wire, send))
        wire = lax.all_to_all(send, "expert", split_axis=0, concat_axis=0, tiled=True)
        count = owners * size
        row_x = wire[:, :size].reshape(count, model_width)
        row_g = wire[:, size : 2 * size].reshape(count, model_width)
        weight = wire[:, 2 * size, 0, :size].reshape(count, 1).astype(jnp.float32)
        gate_pre = jnp.dot(row_x, gate_w, preferred_element_type=jnp.float32)
        up_pre = jnp.dot(row_x, up_w, preferred_element_type=jnp.float32)
        sigmoid_val = jax.nn.sigmoid(gate_pre)
        silu_val = gate_pre * sigmoid_val
        hidden = (silu_val * up_pre).astype(jnp.bfloat16)
        back_grad = jnp.dot(row_g, down_w.T, preferred_element_type=jnp.float32)
        comb_slot = jnp.sum(hidden.astype(jnp.float32) * back_grad, axis=1).astype(jnp.bfloat16)
        hidden_grad = weight * back_grad
        gate_rows_grad = (
            hidden_grad * up_pre * sigmoid_val * (1.0 + gate_pre * (1.0 - sigmoid_val))
        ).astype(jnp.bfloat16)
        up_rows_grad = (hidden_grad * silu_val).astype(jnp.bfloat16)
        scaled_grad = (weight * row_g.astype(jnp.float32)).astype(jnp.bfloat16)
        gate_part = jnp.dot(row_x.T, gate_rows_grad, preferred_element_type=jnp.float32)
        up_part = jnp.dot(row_x.T, up_rows_grad, preferred_element_type=jnp.float32)
        down_part_t = jnp.dot(scaled_grad.T, hidden, preferred_element_type=jnp.float32)
        if gate_acc is None:
            gate_acc, up_acc, down_acc = gate_part, up_part, down_part_t
        else:
            gate_acc, up_acc, down_acc = gate_acc + gate_part, up_acc + up_part, down_acc + down_part_t
        row_grad = (
            jnp.dot(gate_rows_grad, gate_w.T, preferred_element_type=jnp.float32)
            + jnp.dot(up_rows_grad, up_w.T, preferred_element_type=jnp.float32)
        ).astype(jnp.bfloat16)
        comb_tile = jnp.pad(
            comb_slot.reshape(owners, 1, 1, size), ((0, 0), (0, 0), (0, tile_rows - 1), (0, lanes - size))
        )
        back_send = jnp.concatenate([row_grad.reshape(owners, size, tile_rows, lanes), comb_tile], axis=1)
        back = lax.all_to_all(back_send, "expert", split_axis=0, concat_axis=0, tiled=True)
        back_tables.append(back.reshape(owners * (size + 1), tile_rows, lanes))
        back_combs.append(back[:, size, 0, :size])
    parts = jnp.concatenate(
        [gate_acc.astype(jnp.bfloat16), up_acc.astype(jnp.bfloat16), down_acc.astype(jnp.bfloat16)],
        axis=1,
    )
    reduced = lax.psum_scatter(parts, "dp", scatter_dimension=0, tiled=True)
    dest = slot_index // capacity
    pos = slot_index % capacity
    second = chunks[1][1]
    back_index = jnp.where(
        pos < first, dest * (first + 1) + pos, owners * (first + 1) + dest * (second + 1) + pos - first
    )
    back_rows = jnp.concatenate(back_tables, axis=0)[back_index]
    grad_tokens = (
        jnp.sum(back_rows.reshape(tok_dev, fan_out, tile_rows, lanes).astype(jnp.float32), axis=1)
        .astype(jnp.bfloat16)
        .reshape(tok_dev, model_width)
    )
    back_comb = jnp.concatenate(back_combs, axis=1).reshape(slot_count).astype(jnp.float32)
    grad_combine = (
        jnp.sum(jnp.where(hit, back_comb[None, :], 0.0), axis=1).astype(jnp.bfloat16).reshape(tok_dev, fan_out)
    )
    gate_grad = reduced[:, :hidden_units]
    up_grad = reduced[:, hidden_units : 2 * hidden_units]
    down_grad = reduced[:, 2 * hidden_units :].T
    return (
        grad_tokens,
        grad_combine,
        gate_grad[None],
        up_grad[None],
        down_grad[None],
    )


def solution(mesh):
    return jax.shard_map(
        body,
        mesh=mesh,
        in_specs=(
            P(("dp", "expert"), None),
            P(("dp", "expert"), None),
            P(("dp", "expert"), None),
            P(("dp", "expert"), None),
            P("expert", None, None),
            P("expert", None, None),
            P("expert", None, None),
            P(),
        ),
        out_specs=(
            P(("dp", "expert"), None),
            P(("dp", "expert"), None),
            P("expert", "dp", None),
            P("expert", "dp", None),
            P("expert", None, "dp"),
        ),
        check_vma=False,
    )
```

```python
import jax
import jax.numpy as jnp
from jax import lax
from jax.sharding import PartitionSpec as P


def mix_bits(hashed):
    hashed = jnp.bitwise_xor(hashed, jnp.bitwise_and(jnp.right_shift(hashed, 16), 65535))
    hashed = hashed * 2146121005
    hashed = jnp.bitwise_xor(hashed, jnp.bitwise_and(jnp.right_shift(hashed, 15), 131071))
    hashed = hashed * 1284865837
    hashed = jnp.bitwise_xor(hashed, jnp.bitwise_and(jnp.right_shift(hashed, 16), 65535))
    return hashed


def dither(row_block, tok_index, key_word):
    columns = jnp.arange(row_block.shape[1], dtype=jnp.int32)
    salted = mix_bits(key_word + 977)
    keyed_hash = mix_bits(jnp.bitwise_xor(tok_index[:, None] * 4099 + columns[None, :], salted))
    uniform_val = jnp.bitwise_and(keyed_hash, 65535).astype(jnp.float32) * (1.0 / 65536.0)
    values = row_block.astype(jnp.float32)
    magnitude = jnp.abs(values)
    spacing = jnp.full(magnitude.shape, 2.0 ** (-9), jnp.float32)
    for power in range(-5, 9):
        spacing = jnp.where(magnitude >= 2.0**power, spacing * 2.0, spacing)
    rounded = jnp.floor(magnitude / spacing + uniform_val) * spacing
    return jnp.where(values < 0, -rounded, rounded).astype(jnp.bfloat16)


def layer(tokens, grad_out, expert_ids, combine, w_gate, w_up, w_down, dither_keys):
    tok_dev, model_width = tokens.shape
    fan_out = expert_ids.shape[1]
    owners = lax.axis_size("expert")
    capacity = 9 * tok_dev * fan_out // (8 * owners)
    slot_count = owners * capacity
    lanes = 128
    tile_rows = model_width // lanes
    source_block = lax.axis_index("dp") * owners + lax.axis_index("expert")
    tok_index = source_block * tok_dev + jnp.arange(tok_dev, dtype=jnp.int32)
    x_dith = dither(tokens, tok_index, dither_keys[0])
    g_dith = dither(grad_out, tok_index, dither_keys[1])
    flat_ids = expert_ids.reshape(-1)
    onehot = (flat_ids[:, None] == jnp.arange(owners, dtype=jnp.int32)[None, :]).astype(jnp.int32)
    position = jnp.sum((jnp.cumsum(onehot, axis=0) - 1) * onehot, axis=1)
    slot_index = flat_ids * capacity + position
    pair_rows = jnp.arange(tok_dev * fan_out, dtype=jnp.int32)
    hit = slot_index[:, None] == jnp.arange(slot_count, dtype=jnp.int32)[None, :]
    source_row = jnp.min(jnp.where(hit, (pair_rows // fan_out)[:, None], tok_dev), axis=0)
    slot_weight = jnp.sum(
        jnp.where(hit, combine.reshape(-1).astype(jnp.bfloat16).astype(jnp.float32)[:, None], 0.0), axis=0
    ).astype(jnp.bfloat16)
    empty_tile = jnp.zeros((1, tile_rows, lanes), jnp.bfloat16)
    weight_tiles = jnp.pad(
        slot_weight.reshape(owners, 1, capacity), ((0, 0), (0, tile_rows - 1), (0, lanes - capacity))
    )
    table = jnp.concatenate(
        [
            x_dith.reshape(tok_dev, tile_rows, lanes),
            empty_tile,
            g_dith.reshape(tok_dev, tile_rows, lanes),
            empty_tile,
            weight_tiles,
        ],
        axis=0,
    )
    rows_by_dest = source_row.reshape(owners, capacity)
    weight_base = 2 * (tok_dev + 1)
    tile_index = jnp.concatenate(
        [
            rows_by_dest,
            rows_by_dest + (tok_dev + 1),
            weight_base + jnp.arange(owners, dtype=jnp.int32)[:, None],
        ],
        axis=1,
    )
    wire = lax.all_to_all(table[tile_index], "expert", split_axis=0, concat_axis=0, tiled=True)
    row_x = wire[:, :capacity].reshape(slot_count, model_width)
    row_g = wire[:, capacity : 2 * capacity].reshape(slot_count, model_width)
    weight = wire[:, 2 * capacity, 0, :capacity].reshape(slot_count, 1).astype(jnp.float32)
    gate_w = w_gate[0]
    up_w = w_up[0]
    down_w = w_down[0]
    gate_pre = jnp.dot(row_x, gate_w, preferred_element_type=jnp.float32)
    up_pre = jnp.dot(row_x, up_w, preferred_element_type=jnp.float32)
    sigmoid_val = jax.nn.sigmoid(gate_pre)
    silu_val = gate_pre * sigmoid_val
    hidden = (silu_val * up_pre).astype(jnp.bfloat16)
    back_grad = jnp.dot(row_g, down_w.T, preferred_element_type=jnp.float32)
    comb_slot = jnp.sum(hidden.astype(jnp.float32) * back_grad, axis=1).astype(jnp.bfloat16)
    hidden_grad = weight * back_grad
    gate_rows_grad = (
        hidden_grad * up_pre * sigmoid_val * (1.0 + gate_pre * (1.0 - sigmoid_val))
    ).astype(jnp.bfloat16)
    up_rows_grad = (hidden_grad * silu_val).astype(jnp.bfloat16)
    scaled_grad = (weight * row_g.astype(jnp.float32)).astype(jnp.bfloat16)
    row_grad = (
        jnp.dot(gate_rows_grad, gate_w.T, preferred_element_type=jnp.float32)
        + jnp.dot(up_rows_grad, up_w.T, preferred_element_type=jnp.float32)
    ).astype(jnp.bfloat16)
    comb_tile = jnp.pad(
        comb_slot.reshape(owners, 1, 1, capacity), ((0, 0), (0, 0), (0, tile_rows - 1), (0, lanes - capacity))
    )
    back_send = jnp.concatenate(
        [row_grad.reshape(owners, capacity, tile_rows, lanes), comb_tile], axis=1
    )
    back = lax.all_to_all(back_send, "expert", split_axis=0, concat_axis=0, tiled=True)
    gate_part = jnp.dot(row_x.T, gate_rows_grad, preferred_element_type=jnp.float32)
    up_part = jnp.dot(row_x.T, up_rows_grad, preferred_element_type=jnp.float32)
    down_part_t = jnp.dot(scaled_grad.T, hidden, preferred_element_type=jnp.float32)
    parts = jnp.concatenate(
        [gate_part.astype(jnp.bfloat16), up_part.astype(jnp.bfloat16), down_part_t.astype(jnp.bfloat16)],
        axis=1,
    )
    hidden_units = gate_w.shape[1]
    reduced = lax.psum_scatter(parts, "dp", scatter_dimension=0, tiled=True)
    dest = slot_index // capacity
    back_rows = back.reshape(owners * (capacity + 1), tile_rows, lanes)[slot_index + dest]
    grad_tokens = (
        jnp.sum(back_rows.reshape(tok_dev, fan_out, tile_rows, lanes).astype(jnp.float32), axis=1)
        .astype(jnp.bfloat16)
        .reshape(tok_dev, model_width)
    )
    back_comb = back[:, capacity, 0, :capacity].reshape(slot_count).astype(jnp.float32)
    grad_combine = (
        jnp.sum(jnp.where(hit, back_comb[None, :], 0.0), axis=1).astype(jnp.bfloat16).reshape(tok_dev, fan_out)
    )
    gate_grad = reduced[:, :hidden_units]
    up_grad = reduced[:, hidden_units : 2 * hidden_units]
    down_grad = reduced[:, 2 * hidden_units :].T
    return (
        grad_tokens,
        grad_combine,
        gate_grad[None],
        up_grad[None],
        down_grad[None],
    )


def solution(mesh):
    return jax.shard_map(
        layer,
        mesh=mesh,
        in_specs=(
            P(("dp", "expert"), None),
            P(("dp", "expert"), None),
            P(("dp", "expert"), None),
            P(("dp", "expert"), None),
            P("expert", None, None),
            P("expert", None, None),
            P("expert", None, None),
            P(),
        ),
        out_specs=(
            P(("dp", "expert"), None),
            P(("dp", "expert"), None),
            P("expert", "dp", None),
            P("expert", "dp", None),
            P("expert", None, "dp"),
        ),
        check_vma=False,
    )
```

```python
import jax
import jax.numpy as jnp
from jax import lax
from jax.sharding import PartitionSpec as P


def mix_bits(hashed):
    hashed = jnp.bitwise_xor(hashed, jnp.bitwise_and(jnp.right_shift(hashed, 16), 65535))
    hashed = hashed * 2146121005
    hashed = jnp.bitwise_xor(hashed, jnp.bitwise_and(jnp.right_shift(hashed, 15), 131071))
    hashed = hashed * 1284865837
    hashed = jnp.bitwise_xor(hashed, jnp.bitwise_and(jnp.right_shift(hashed, 16), 65535))
    return hashed


def dither(row_block, tok_index, key_word):
    columns = jnp.arange(row_block.shape[1], dtype=jnp.int32)
    salted = mix_bits(key_word + 977)
    keyed_hash = mix_bits(jnp.bitwise_xor(tok_index[:, None] * 4099 + columns[None, :], salted))
    uniform_val = jnp.bitwise_and(keyed_hash, 65535).astype(jnp.float32) * (1.0 / 65536.0)
    values = row_block.astype(jnp.float32)
    magnitude = jnp.abs(values)
    spacing = jnp.full(magnitude.shape, 2.0 ** (-9), jnp.float32)
    for power in range(-5, 9):
        spacing = jnp.where(magnitude >= 2.0**power, spacing * 2.0, spacing)
    rounded = jnp.floor(magnitude / spacing + uniform_val) * spacing
    return jnp.where(values < 0, -rounded, rounded).astype(jnp.bfloat16)


def body(tokens, grad_out, expert_ids, combine, w_gate, w_up, w_down, dither_keys):
    tok_dev, model_width = tokens.shape
    fan_out = expert_ids.shape[1]
    owners = lax.axis_size("expert")
    capacity = 9 * tok_dev * fan_out // (8 * owners)
    slot_count = owners * capacity
    lanes = 128
    tile_rows = model_width // lanes
    source_block = lax.axis_index("dp") * owners + lax.axis_index("expert")
    tok_index = source_block * tok_dev + jnp.arange(tok_dev, dtype=jnp.int32)
    x_dith = dither(tokens, tok_index, dither_keys[0])
    g_dith = dither(grad_out, tok_index, dither_keys[1])
    flat_ids = expert_ids.reshape(-1)
    onehot = (flat_ids[:, None] == jnp.arange(owners, dtype=jnp.int32)[None, :]).astype(jnp.int32)
    position = jnp.sum((jnp.cumsum(onehot, axis=0) - 1) * onehot, axis=1)
    slot_index = flat_ids * capacity + position
    pair_rows = jnp.arange(tok_dev * fan_out, dtype=jnp.int32)
    hit = slot_index[:, None] == jnp.arange(slot_count, dtype=jnp.int32)[None, :]
    source_row = jnp.min(jnp.where(hit, (pair_rows // fan_out)[:, None], tok_dev), axis=0)
    slot_weight = jnp.sum(
        jnp.where(hit, combine.reshape(-1).astype(jnp.bfloat16).astype(jnp.float32)[:, None], 0.0), axis=0
    ).astype(jnp.bfloat16)
    empty_tile = jnp.zeros((1, tile_rows, lanes), jnp.bfloat16)
    weight_tiles = jnp.pad(
        slot_weight.reshape(owners, 1, capacity), ((0, 0), (0, tile_rows - 1), (0, lanes - capacity))
    )
    table = jnp.concatenate(
        [
            x_dith.reshape(tok_dev, tile_rows, lanes),
            empty_tile,
            g_dith.reshape(tok_dev, tile_rows, lanes),
            empty_tile,
            weight_tiles,
        ],
        axis=0,
    )
    rows_by_dest = source_row.reshape(owners, capacity)
    weight_base = 2 * (tok_dev + 1)
    tile_index = jnp.concatenate(
        [
            rows_by_dest,
            rows_by_dest + (tok_dev + 1),
            weight_base + jnp.arange(owners, dtype=jnp.int32)[:, None],
        ],
        axis=1,
    )
    wire = lax.all_to_all(table[tile_index], "expert", split_axis=0, concat_axis=0, tiled=True)
    row_x = wire[:, :capacity].reshape(slot_count, model_width)
    row_g = wire[:, capacity : 2 * capacity].reshape(slot_count, model_width)
    weight = wire[:, 2 * capacity, 0, :capacity].reshape(slot_count, 1).astype(jnp.float32)
    gate_w = w_gate[0]
    up_w = w_up[0]
    down_w = w_down[0]
    gate_pre = jnp.dot(row_x, gate_w, preferred_element_type=jnp.float32)
    up_pre = jnp.dot(row_x, up_w, preferred_element_type=jnp.float32)
    sigmoid_val = jax.nn.sigmoid(gate_pre)
    silu_val = gate_pre * sigmoid_val
    hidden = (silu_val * up_pre).astype(jnp.bfloat16)
    back_grad = jnp.dot(row_g, down_w.T, preferred_element_type=jnp.float32)
    comb_slot = jnp.sum(hidden.astype(jnp.float32) * back_grad, axis=1).astype(jnp.bfloat16)
    hidden_grad = weight * back_grad
    gate_rows_grad = (
        hidden_grad * up_pre * sigmoid_val * (1.0 + gate_pre * (1.0 - sigmoid_val))
    ).astype(jnp.bfloat16)
    up_rows_grad = (hidden_grad * silu_val).astype(jnp.bfloat16)
    scaled_grad = (weight * row_g.astype(jnp.float32)).astype(jnp.bfloat16)
    row_grad = (
        jnp.dot(gate_rows_grad, gate_w.T, preferred_element_type=jnp.float32)
        + jnp.dot(up_rows_grad, up_w.T, preferred_element_type=jnp.float32)
    ).astype(jnp.bfloat16)
    comb_tile = jnp.pad(
        comb_slot.reshape(owners, 1, 1, capacity), ((0, 0), (0, 0), (0, tile_rows - 1), (0, lanes - capacity))
    )
    back_send = jnp.concatenate(
        [row_grad.reshape(owners, capacity, tile_rows, lanes), comb_tile], axis=1
    )
    back = lax.all_to_all(back_send, "expert", split_axis=0, concat_axis=0, tiled=True)
    gate_part = jnp.dot(row_x.T, gate_rows_grad, preferred_element_type=jnp.float32)
    up_part = jnp.dot(row_x.T, up_rows_grad, preferred_element_type=jnp.float32)
    down_part_t = jnp.dot(scaled_grad.T, hidden, preferred_element_type=jnp.float32)
    parts = jnp.stack(
        [gate_part.astype(jnp.bfloat16), up_part.astype(jnp.bfloat16), down_part_t.astype(jnp.bfloat16)]
    )
    reduced = lax.psum_scatter(parts, "dp", scatter_dimension=1, tiled=True)
    dest = slot_index // capacity
    back_rows = back.reshape(owners * (capacity + 1), tile_rows, lanes)[slot_index + dest]
    grad_tokens = (
        jnp.sum(back_rows.reshape(tok_dev, fan_out, tile_rows, lanes).astype(jnp.float32), axis=1)
        .astype(jnp.bfloat16)
        .reshape(tok_dev, model_width)
    )
    back_comb = back[:, capacity, 0, :capacity].reshape(slot_count).astype(jnp.float32)
    grad_combine = (
        jnp.sum(jnp.where(hit, back_comb[None, :], 0.0), axis=1).astype(jnp.bfloat16).reshape(tok_dev, fan_out)
    )
    gate_grad = reduced[0]
    up_grad = reduced[1]
    down_grad = reduced[2].T
    return (
        grad_tokens,
        grad_combine,
        gate_grad[None],
        up_grad[None],
        down_grad[None],
    )


def solution(mesh):
    return jax.shard_map(
        body,
        mesh=mesh,
        in_specs=(
            P(("dp", "expert"), None),
            P(("dp", "expert"), None),
            P(("dp", "expert"), None),
            P(("dp", "expert"), None),
            P("expert", None, None),
            P("expert", None, None),
            P("expert", None, None),
            P(),
        ),
        out_specs=(
            P(("dp", "expert"), None),
            P(("dp", "expert"), None),
            P("expert", "dp", None),
            P("expert", "dp", None),
            P("expert", None, "dp"),
        ),
        check_vma=False,
    )
```

```python
import jax
import jax.numpy as jnp
from jax import lax
from jax.sharding import PartitionSpec as P


def mix_bits(hashed):
    hashed = jnp.bitwise_xor(hashed, jnp.bitwise_and(jnp.right_shift(hashed, 16), 65535))
    hashed = hashed * 2146121005
    hashed = jnp.bitwise_xor(hashed, jnp.bitwise_and(jnp.right_shift(hashed, 15), 131071))
    hashed = hashed * 1284865837
    hashed = jnp.bitwise_xor(hashed, jnp.bitwise_and(jnp.right_shift(hashed, 16), 65535))
    return hashed


def dither(row_block, tok_index, key_word):
    columns = jnp.arange(row_block.shape[1], dtype=jnp.int32)
    salted = mix_bits(key_word + 977)
    keyed_hash = mix_bits(jnp.bitwise_xor(tok_index[:, None] * 4099 + columns[None, :], salted))
    uniform_val = jnp.bitwise_and(keyed_hash, 65535).astype(jnp.float32) * (1.0 / 65536.0)
    values = row_block.astype(jnp.float32)
    magnitude = jnp.abs(values)
    spacing = jnp.full(magnitude.shape, 2.0 ** (-9), jnp.float32)
    for power in range(-5, 9):
        spacing = jnp.where(magnitude >= 2.0**power, spacing * 2.0, spacing)
    rounded = jnp.floor(magnitude / spacing + uniform_val) * spacing
    return jnp.where(values < 0, -rounded, rounded).astype(jnp.bfloat16)


def body(tokens, grad_out, expert_ids, combine, w_gate, w_up, w_down, dither_keys):
    tok_dev, model_width = tokens.shape
    fan_out = expert_ids.shape[1]
    owners = lax.axis_size("expert")
    capacity = 9 * tok_dev * fan_out // (8 * owners)
    slot_count = owners * capacity
    lanes = 128
    tile_rows = model_width // lanes
    source_block = lax.axis_index("dp") * owners + lax.axis_index("expert")
    tok_index = source_block * tok_dev + jnp.arange(tok_dev, dtype=jnp.int32)
    x_dith = dither(tokens, tok_index, dither_keys[0])
    g_dith = dither(grad_out, tok_index, dither_keys[1])
    flat_ids = expert_ids.reshape(-1)
    onehot = (flat_ids[:, None] == jnp.arange(owners, dtype=jnp.int32)[None, :]).astype(jnp.int32)
    position = jnp.sum((jnp.cumsum(onehot, axis=0) - 1) * onehot, axis=1)
    slot_index = flat_ids * capacity + position
    pair_rows = jnp.arange(tok_dev * fan_out, dtype=jnp.int32)
    hit = slot_index[:, None] == jnp.arange(slot_count, dtype=jnp.int32)[None, :]
    source_row = jnp.min(jnp.where(hit, (pair_rows // fan_out)[:, None], tok_dev), axis=0)
    slot_weight = jnp.sum(
        jnp.where(hit, combine.reshape(-1).astype(jnp.bfloat16).astype(jnp.float32)[:, None], 0.0), axis=0
    ).astype(jnp.bfloat16)
    empty_tile = jnp.zeros((1, tile_rows, lanes), jnp.bfloat16)
    weight_tiles = jnp.pad(
        slot_weight.reshape(owners, 1, capacity), ((0, 0), (0, tile_rows - 1), (0, lanes - capacity))
    )
    table = jnp.concatenate(
        [
            x_dith.reshape(tok_dev, tile_rows, lanes),
            empty_tile,
            g_dith.reshape(tok_dev, tile_rows, lanes),
            empty_tile,
            weight_tiles,
        ],
        axis=0,
    )
    rows_by_dest = source_row.reshape(owners, capacity)
    weight_base = 2 * (tok_dev + 1)
    tile_index = jnp.concatenate(
        [
            rows_by_dest,
            rows_by_dest + (tok_dev + 1),
            weight_base + jnp.arange(owners, dtype=jnp.int32)[:, None],
        ],
        axis=1,
    )
    wire = lax.all_to_all(table[tile_index], "expert", split_axis=0, concat_axis=0, tiled=True)
    row_x = wire[:, :capacity].reshape(slot_count, model_width)
    row_g = wire[:, capacity : 2 * capacity].reshape(slot_count, model_width)
    weight = wire[:, 2 * capacity, 0, :capacity].reshape(slot_count, 1).astype(jnp.float32)
    gate_w = w_gate[0]
    up_w = w_up[0]
    down_w = w_down[0]
    gate_pre = jnp.dot(row_x, gate_w, preferred_element_type=jnp.float32)
    up_pre = jnp.dot(row_x, up_w, preferred_element_type=jnp.float32)
    sigmoid_val = jax.nn.sigmoid(gate_pre)
    silu_val = gate_pre * sigmoid_val
    hidden = (silu_val * up_pre).astype(jnp.bfloat16)
    back_grad = jnp.dot(row_g, down_w.T, preferred_element_type=jnp.float32)
    comb_slot = jnp.sum(hidden.astype(jnp.float32) * back_grad, axis=1).astype(jnp.bfloat16)
    hidden_grad = weight * back_grad
    gate_rows_grad = (
        hidden_grad * up_pre * sigmoid_val * (1.0 + gate_pre * (1.0 - sigmoid_val))
    ).astype(jnp.bfloat16)
    up_rows_grad = (hidden_grad * silu_val).astype(jnp.bfloat16)
    scaled_grad = (weight * row_g.astype(jnp.float32)).astype(jnp.bfloat16)
    row_grad = (
        jnp.dot(gate_rows_grad, gate_w.T, preferred_element_type=jnp.float32)
        + jnp.dot(up_rows_grad, up_w.T, preferred_element_type=jnp.float32)
    ).astype(jnp.bfloat16)
    comb_tile = jnp.pad(
        comb_slot.reshape(owners, 1, 1, capacity), ((0, 0), (0, 0), (0, tile_rows - 1), (0, lanes - capacity))
    )
    back_send = jnp.concatenate(
        [row_grad.reshape(owners, capacity, tile_rows, lanes), comb_tile], axis=1
    )
    back = lax.all_to_all(back_send, "expert", split_axis=0, concat_axis=0, tiled=True)
    gate_part = jnp.dot(row_x.T, gate_rows_grad, preferred_element_type=jnp.float32)
    up_part = jnp.dot(row_x.T, up_rows_grad, preferred_element_type=jnp.float32)
    down_part_t = jnp.dot(scaled_grad.T, hidden, preferred_element_type=jnp.float32)
    parts = jnp.stack(
        [gate_part.astype(jnp.bfloat16), up_part.astype(jnp.bfloat16), down_part_t.astype(jnp.bfloat16)]
    )
    reduced = lax.psum_scatter(parts, "dp", scatter_dimension=1, tiled=True)
    dest = slot_index // capacity
    returned = jnp.arange(owners * (capacity + 1), dtype=jnp.int32)
    token_of = jnp.where(
        (slot_index + dest)[None, :] == returned[:, None], (pair_rows // fan_out)[None, :], tok_dev
    ).min(axis=1)
    gather_matrix = (jnp.arange(tok_dev, dtype=jnp.int32)[:, None] == token_of[None, :]).astype(jnp.bfloat16)
    grad_tokens = jnp.dot(
        gather_matrix, back.reshape(owners * (capacity + 1), model_width), preferred_element_type=jnp.float32
    ).astype(jnp.bfloat16)
    back_comb = back[:, capacity, 0, :capacity].reshape(slot_count).astype(jnp.float32)
    grad_combine = (
        jnp.sum(jnp.where(hit, back_comb[None, :], 0.0), axis=1).astype(jnp.bfloat16).reshape(tok_dev, fan_out)
    )
    gate_grad = reduced[0]
    up_grad = reduced[1]
    down_grad = reduced[2].T
    return (
        grad_tokens,
        grad_combine,
        gate_grad[None],
        up_grad[None],
        down_grad[None],
    )


def solution(mesh):
    return jax.shard_map(
        body,
        mesh=mesh,
        in_specs=(
            P(("dp", "expert"), None),
            P(("dp", "expert"), None),
            P(("dp", "expert"), None),
            P(("dp", "expert"), None),
            P("expert", None, None),
            P("expert", None, None),
            P("expert", None, None),
            P(),
        ),
        out_specs=(
            P(("dp", "expert"), None),
            P(("dp", "expert"), None),
            P("expert", "dp", None),
            P("expert", "dp", None),
            P("expert", None, "dp"),
        ),
        check_vma=False,
    )
```

```python
import jax
import jax.numpy as jnp
from jax import lax
from jax.sharding import PartitionSpec as P


def mix_bits(hashed):
    hashed = jnp.bitwise_xor(hashed, jnp.bitwise_and(jnp.right_shift(hashed, 16), 65535))
    hashed = hashed * 2146121005
    hashed = jnp.bitwise_xor(hashed, jnp.bitwise_and(jnp.right_shift(hashed, 15), 131071))
    hashed = hashed * 1284865837
    hashed = jnp.bitwise_xor(hashed, jnp.bitwise_and(jnp.right_shift(hashed, 16), 65535))
    return hashed


def dither(row_block, tok_index, key_word):
    columns = jnp.arange(row_block.shape[1], dtype=jnp.int32)
    salted = mix_bits(key_word + 977)
    keyed_hash = mix_bits(jnp.bitwise_xor(tok_index[:, None] * 4099 + columns[None, :], salted))
    uniform_val = jnp.bitwise_and(keyed_hash, 65535).astype(jnp.float32) * (1.0 / 65536.0)
    values = row_block.astype(jnp.float32)
    magnitude = jnp.abs(values)
    spacing = jnp.full(magnitude.shape, 2.0 ** (-9), jnp.float32)
    for power in range(-5, 9):
        spacing = jnp.where(magnitude >= 2.0**power, spacing * 2.0, spacing)
    rounded = jnp.floor(magnitude / spacing + uniform_val) * spacing
    return jnp.where(values < 0, -rounded, rounded).astype(jnp.bfloat16)


def body(tokens, grad_out, expert_ids, combine, w_gate, w_up, w_down, dither_keys):
    tok_dev, model_width = tokens.shape
    fan_out = expert_ids.shape[1]
    owners = lax.axis_size("expert")
    capacity = 9 * tok_dev * fan_out // (8 * owners)
    slot_count = owners * capacity
    lanes = 128
    tile_rows = model_width // lanes
    source_block = lax.axis_index("dp") * owners + lax.axis_index("expert")
    tok_index = source_block * tok_dev + jnp.arange(tok_dev, dtype=jnp.int32)
    x_dith = dither(tokens, tok_index, dither_keys[0])
    g_dith = dither(grad_out, tok_index, dither_keys[1])
    flat_ids = expert_ids.reshape(-1)
    onehot = (flat_ids[:, None] == jnp.arange(owners, dtype=jnp.int32)[None, :]).astype(jnp.int32)
    position = jnp.sum((jnp.cumsum(onehot, axis=0) - 1) * onehot, axis=1)
    slot_index = flat_ids * capacity + position
    pair_rows = jnp.arange(tok_dev * fan_out, dtype=jnp.int32)
    hit = slot_index[:, None] == jnp.arange(slot_count, dtype=jnp.int32)[None, :]
    source_row = jnp.min(jnp.where(hit, (pair_rows // fan_out)[:, None], tok_dev), axis=0)
    slot_weight = jnp.sum(
        jnp.where(hit, combine.reshape(-1).astype(jnp.bfloat16).astype(jnp.float32)[:, None], 0.0), axis=0
    ).astype(jnp.bfloat16)
    empty_tile = jnp.zeros((1, tile_rows, lanes), jnp.bfloat16)
    weight_tiles = jnp.pad(
        slot_weight.reshape(owners, 1, capacity), ((0, 0), (0, tile_rows - 1), (0, lanes - capacity))
    )
    table = jnp.concatenate(
        [
            x_dith.reshape(tok_dev, tile_rows, lanes),
            empty_tile,
            g_dith.reshape(tok_dev, tile_rows, lanes),
            empty_tile,
            weight_tiles,
        ],
        axis=0,
    )
    rows_by_dest = source_row.reshape(owners, capacity)
    weight_base = 2 * (tok_dev + 1)
    tile_index = jnp.concatenate(
        [
            rows_by_dest,
            rows_by_dest + (tok_dev + 1),
            weight_base + jnp.arange(owners, dtype=jnp.int32)[:, None],
        ],
        axis=1,
    )
    wire = lax.all_to_all(table[tile_index], "expert", split_axis=0, concat_axis=0, tiled=True)
    row_x = wire[:, :capacity].reshape(slot_count, model_width)
    row_g = wire[:, capacity : 2 * capacity].reshape(slot_count, model_width)
    weight = wire[:, 2 * capacity, 0, :capacity].reshape(slot_count, 1).astype(jnp.float32)
    gate_w = w_gate[0]
    up_w = w_up[0]
    down_w = w_down[0]
    gate_pre = jnp.dot(row_x, gate_w, preferred_element_type=jnp.float32)
    up_pre = jnp.dot(row_x, up_w, preferred_element_type=jnp.float32)
    sigmoid_val = jax.nn.sigmoid(gate_pre)
    silu_val = gate_pre * sigmoid_val
    hidden = (silu_val * up_pre).astype(jnp.bfloat16)
    back_grad = jnp.dot(row_g, down_w.T, preferred_element_type=jnp.float32)
    comb_slot = jnp.sum(hidden.astype(jnp.float32) * back_grad, axis=1).astype(jnp.bfloat16)
    hidden_grad = weight * back_grad
    gate_rows_grad = (
        hidden_grad * up_pre * sigmoid_val * (1.0 + gate_pre * (1.0 - sigmoid_val))
    ).astype(jnp.bfloat16)
    up_rows_grad = (hidden_grad * silu_val).astype(jnp.bfloat16)
    scaled_grad = (weight * row_g.astype(jnp.float32)).astype(jnp.bfloat16)
    row_grad = (
        jnp.dot(gate_rows_grad, gate_w.T, preferred_element_type=jnp.float32)
        + jnp.dot(up_rows_grad, up_w.T, preferred_element_type=jnp.float32)
    ).astype(jnp.bfloat16)
    comb_tile = jnp.pad(
        comb_slot.reshape(owners, 1, 1, capacity), ((0, 0), (0, 0), (0, tile_rows - 1), (0, lanes - capacity))
    )
    back_send = jnp.concatenate(
        [row_grad.reshape(owners, capacity, tile_rows, lanes), comb_tile], axis=1
    )
    back = lax.all_to_all(back_send, "expert", split_axis=0, concat_axis=0, tiled=True)
    parts = lax.dot_general(
        jnp.stack([row_x, row_x, scaled_grad]),
        jnp.stack([gate_rows_grad, up_rows_grad, hidden]),
        (((1,), (1,)), ((0,), (0,))),
        preferred_element_type=jnp.float32,
    ).astype(jnp.bfloat16)
    reduced = lax.psum_scatter(parts, "dp", scatter_dimension=1, tiled=True)
    dest = slot_index // capacity
    returned = jnp.arange(owners * (capacity + 1), dtype=jnp.int32)
    token_of = jnp.where(
        (slot_index + dest)[None, :] == returned[:, None], (pair_rows // fan_out)[None, :], tok_dev
    ).min(axis=1)
    gather_matrix = (jnp.arange(tok_dev, dtype=jnp.int32)[:, None] == token_of[None, :]).astype(jnp.bfloat16)
    grad_tokens = jnp.dot(
        gather_matrix, back.reshape(owners * (capacity + 1), model_width), preferred_element_type=jnp.float32
    ).astype(jnp.bfloat16)
    back_comb = back[:, capacity, 0, :capacity].reshape(slot_count).astype(jnp.float32)
    grad_combine = (
        jnp.sum(jnp.where(hit, back_comb[None, :], 0.0), axis=1).astype(jnp.bfloat16).reshape(tok_dev, fan_out)
    )
    gate_grad = reduced[0]
    up_grad = reduced[1]
    down_grad = reduced[2].T
    return (
        grad_tokens,
        grad_combine,
        gate_grad[None],
        up_grad[None],
        down_grad[None],
    )


def solution(mesh):
    return jax.shard_map(
        body,
        mesh=mesh,
        in_specs=(
            P(("dp", "expert"), None),
            P(("dp", "expert"), None),
            P(("dp", "expert"), None),
            P(("dp", "expert"), None),
            P("expert", None, None),
            P("expert", None, None),
            P("expert", None, None),
            P(),
        ),
        out_specs=(
            P(("dp", "expert"), None),
            P(("dp", "expert"), None),
            P("expert", "dp", None),
            P("expert", "dp", None),
            P("expert", None, "dp"),
        ),
        check_vma=False,
    )
```

```python
import jax
import jax.numpy as jnp
from jax import lax
from jax.sharding import PartitionSpec as P


def mix_bits(hashed):
    hashed = jnp.bitwise_xor(hashed, jnp.bitwise_and(jnp.right_shift(hashed, 16), 65535))
    hashed = hashed * 2146121005
    hashed = jnp.bitwise_xor(hashed, jnp.bitwise_and(jnp.right_shift(hashed, 15), 131071))
    hashed = hashed * 1284865837
    hashed = jnp.bitwise_xor(hashed, jnp.bitwise_and(jnp.right_shift(hashed, 16), 65535))
    return hashed


def dither(row_block, tok_index, key_word):
    columns = jnp.arange(row_block.shape[1], dtype=jnp.int32)
    salted = mix_bits(key_word + 977)
    keyed_hash = mix_bits(jnp.bitwise_xor(tok_index[:, None] * 4099 + columns[None, :], salted))
    uniform_val = jnp.bitwise_and(keyed_hash, 65535).astype(jnp.float32) * (1.0 / 65536.0)
    values = row_block.astype(jnp.float32)
    magnitude = jnp.abs(values)
    spacing = jnp.full(magnitude.shape, 2.0 ** (-9), jnp.float32)
    for power in range(-5, 9):
        spacing = jnp.where(magnitude >= 2.0**power, spacing * 2.0, spacing)
    rounded = jnp.floor(magnitude / spacing + uniform_val) * spacing
    return jnp.where(values < 0, -rounded, rounded).astype(jnp.bfloat16)


def body(tokens, grad_out, expert_ids, combine, w_gate, w_up, w_down, dither_keys):
    tok_dev, model_width = tokens.shape
    fan_out = expert_ids.shape[1]
    owners = lax.axis_size("expert")
    capacity = 9 * tok_dev * fan_out // (8 * owners)
    slot_count = owners * capacity
    lanes = 128
    tile_rows = model_width // lanes
    source_block = lax.axis_index("dp") * owners + lax.axis_index("expert")
    tok_index = source_block * tok_dev + jnp.arange(tok_dev, dtype=jnp.int32)
    both_dith = dither(
        jnp.concatenate([tokens, grad_out], axis=0),
        jnp.concatenate([tok_index, tok_index]),
        jnp.repeat(dither_keys[:2], tok_dev)[:, None],
    )
    flat_ids = expert_ids.reshape(-1)
    onehot = (flat_ids[:, None] == jnp.arange(owners, dtype=jnp.int32)[None, :]).astype(jnp.int32)
    position = jnp.sum((jnp.cumsum(onehot, axis=0) - 1) * onehot, axis=1)
    slot_index = flat_ids * capacity + position
    pair_rows = jnp.arange(tok_dev * fan_out, dtype=jnp.int32)
    hit = slot_index[:, None] == jnp.arange(slot_count, dtype=jnp.int32)[None, :]
    source_row = jnp.min(jnp.where(hit, (pair_rows // fan_out)[:, None], tok_dev), axis=0)
    slot_weight = jnp.sum(
        jnp.where(hit, combine.reshape(-1).astype(jnp.bfloat16).astype(jnp.float32)[:, None], 0.0), axis=0
    ).astype(jnp.bfloat16)
    empty_tile = jnp.zeros((1, tile_rows, lanes), jnp.bfloat16)
    weight_tiles = jnp.pad(
        slot_weight.reshape(owners, 1, capacity), ((0, 0), (0, tile_rows - 1), (0, lanes - capacity))
    )
    table = jnp.concatenate(
        [both_dith.reshape(2 * tok_dev, tile_rows, lanes), weight_tiles, empty_tile], axis=0
    )
    rows_by_dest = source_row.reshape(owners, capacity)
    empty_index = 2 * tok_dev + owners
    tile_index = jnp.concatenate(
        [
            jnp.where(rows_by_dest == tok_dev, empty_index, rows_by_dest),
            jnp.where(rows_by_dest == tok_dev, empty_index, rows_by_dest + tok_dev),
            2 * tok_dev + jnp.arange(owners, dtype=jnp.int32)[:, None],
        ],
        axis=1,
    )
    wire = lax.all_to_all(table[tile_index], "expert", split_axis=0, concat_axis=0, tiled=True)
    row_x = wire[:, :capacity].reshape(slot_count, model_width)
    row_g = wire[:, capacity : 2 * capacity].reshape(slot_count, model_width)
    weight = wire[:, 2 * capacity, 0, :capacity].reshape(slot_count, 1).astype(jnp.float32)
    gate_w = w_gate[0]
    up_w = w_up[0]
    down_w = w_down[0]
    gate_pre = jnp.dot(row_x, gate_w, preferred_element_type=jnp.float32)
    up_pre = jnp.dot(row_x, up_w, preferred_element_type=jnp.float32)
    sigmoid_val = jax.nn.sigmoid(gate_pre)
    silu_val = gate_pre * sigmoid_val
    hidden = (silu_val * up_pre).astype(jnp.bfloat16)
    back_grad = jnp.dot(row_g, down_w.T, preferred_element_type=jnp.float32)
    comb_slot = jnp.sum(hidden.astype(jnp.float32) * back_grad, axis=1).astype(jnp.bfloat16)
    hidden_grad = weight * back_grad
    gate_rows_grad = (
        hidden_grad * up_pre * sigmoid_val * (1.0 + gate_pre * (1.0 - sigmoid_val))
    ).astype(jnp.bfloat16)
    up_rows_grad = (hidden_grad * silu_val).astype(jnp.bfloat16)
    scaled_grad = (weight * row_g.astype(jnp.float32)).astype(jnp.bfloat16)
    row_grad = (
        jnp.dot(gate_rows_grad, gate_w.T, preferred_element_type=jnp.float32)
        + jnp.dot(up_rows_grad, up_w.T, preferred_element_type=jnp.float32)
    ).astype(jnp.bfloat16)
    comb_tile = jnp.pad(
        comb_slot.reshape(owners, 1, 1, capacity), ((0, 0), (0, 0), (0, tile_rows - 1), (0, lanes - capacity))
    )
    back_send = jnp.concatenate(
        [row_grad.reshape(owners, capacity, tile_rows, lanes), comb_tile], axis=1
    )
    back = lax.all_to_all(back_send, "expert", split_axis=0, concat_axis=0, tiled=True)
    gate_part = jnp.dot(row_x.T, gate_rows_grad, preferred_element_type=jnp.float32)
    up_part = jnp.dot(row_x.T, up_rows_grad, preferred_element_type=jnp.float32)
    down_part_t = jnp.dot(scaled_grad.T, hidden, preferred_element_type=jnp.float32)
    parts = jnp.stack(
        [gate_part.astype(jnp.bfloat16), up_part.astype(jnp.bfloat16), down_part_t.astype(jnp.bfloat16)]
    )
    reduced = lax.psum_scatter(parts, "dp", scatter_dimension=1, tiled=True)
    dest = slot_index // capacity
    returned = jnp.arange(owners * (capacity + 1), dtype=jnp.int32)
    token_of = jnp.where(
        (slot_index + dest)[None, :] == returned[:, None], (pair_rows // fan_out)[None, :], tok_dev
    ).min(axis=1)
    gather_matrix = (jnp.arange(tok_dev, dtype=jnp.int32)[:, None] == token_of[None, :]).astype(jnp.bfloat16)
    grad_tokens = jnp.dot(
        gather_matrix, back.reshape(owners * (capacity + 1), model_width), preferred_element_type=jnp.float32
    ).astype(jnp.bfloat16)
    back_comb = back[:, capacity, 0, :capacity].reshape(slot_count).astype(jnp.float32)
    grad_combine = (
        jnp.sum(jnp.where(hit, back_comb[None, :], 0.0), axis=1).astype(jnp.bfloat16).reshape(tok_dev, fan_out)
    )
    gate_grad = reduced[0]
    up_grad = reduced[1]
    down_grad = reduced[2].T
    return (
        grad_tokens,
        grad_combine,
        gate_grad[None],
        up_grad[None],
        down_grad[None],
    )


def solution(mesh):
    return jax.shard_map(
        body,
        mesh=mesh,
        in_specs=(
            P(("dp", "expert"), None),
            P(("dp", "expert"), None),
            P(("dp", "expert"), None),
            P(("dp", "expert"), None),
            P("expert", None, None),
            P("expert", None, None),
            P("expert", None, None),
            P(),
        ),
        out_specs=(
            P(("dp", "expert"), None),
            P(("dp", "expert"), None),
            P("expert", "dp", None),
            P("expert", "dp", None),
            P("expert", None, "dp"),
        ),
        check_vma=False,
    )
```
